768 devices in a mesh: row: 192 (over z_lo, y, x, core), col: 4 (over z_hi).
Axes of the slice: x: 4, y: 8, z: 12 (z_hi: 4, z_lo: 3; z = z_hi * 3 + z_lo), core: 2. Of those that a mesh axis runs over, the one named last changes fastest.
Arguments:
- features: bfloat16 [98304, 512], P('row', 'col'), may hold values from -6 to 6
- out_grad: bfloat16 [98304, 512], P('row', 'col'), may hold values from -6 to 6
- self_weight: bfloat16 [512, 512], replicated, may hold values from -0.25 to 0.25
- neigh_weight: bfloat16 [512, 512], replicated, may hold values from -1 to 1
- tile_rows: int32 [98304, 16, 128], P('row'), may hold values from 0 to 1, as said below
- tile_cols: int32 [98304, 16], P('row'), may hold values from 0 to 767, as said below
- degree: int32 [98304], P('row'), may hold values from 32 to 512
Outputs:
- output: bfloat16 [98304, 512], P('row', 'col')
- feature_grad: bfloat16 [98304, 512], P('row', 'col')
The draws below stay inside these ranges and needn't reach their ends.
Inputs may be any that keep to these rules, and one draw needn't show every extreme that they name: Entries are 0 or 1. The adjacency built from tile_rows and tile_cols is symmetric. All nodes of one block of 128 nodes have the same tile_cols. A slot that is not used holds an all-zero tile. `tile_cols`: for each slot, block a names block b exactly when block b names block a; b differs from a by 1 or 2, or b equals a and that slot's tile is all zero.
All inputs are finite; a program needn't handle non-finite values.
Results may differ from the reference program's by a relative error of at most 0.0034.
Values may be sent and summed in bfloat16 or wider, within the bound.
No kernel may reach another device: no remote copies, remote signals or barrier semaphores. Data moves between devices by JAX's collectives and lax.ppermute only.
A program may use at most 128 MiB of HBM per device.

```python
import jax
import jax.numpy as jnp
from jax import lax

WIDTH = 512
BLOCK = 128
SLOTS = 16
ROWS_DEV = 512
NODES = 98304
N_ROW = 192


def adjacency_parts(key):
    nodes = ROWS_DEV * N_ROW
    blocks = nodes // BLOCK
    start = jax.random.randint(jax.random.fold_in(key, 11), (), 0, 2).astype(jnp.int32)
    order = jax.random.permutation(jax.random.fold_in(key, 14), SLOTS).astype(jnp.int32)
    role = order[:, None]
    reach = 1 + (role + start) % 2
    occurrence = role // 2
    first_bits = jax.random.randint(jax.random.fold_in(key, 16), (2,), 0, 2).astype(jnp.int32)
    spare_bits = jax.random.randint(jax.random.fold_in(key, 15), (SLOTS, 1), 0, 2).astype(jnp.int32)
    base_bit = first_bits[reach - 1]
    phase_bit = jnp.where(occurrence == 0, base_bit, jnp.where(occurrence == 1, 1 - base_bit, spare_bits))
    phase = reach * phase_bit
    own = jnp.arange(blocks, dtype=jnp.int32)[None, :]
    upward = (own + phase) // reach % 2 == 0
    partner = jnp.where(upward, own + reach, own - reach).astype(jnp.int32)
    inside = (partner >= 0) & (partner < blocks)
    partner = jnp.where(inside, partner, own).astype(jnp.int32)
    least = min(SLOTS, max(4, SLOTS // 2))
    capacity = jax.random.randint(jax.random.fold_in(key, 12), (blocks,), least, SLOTS + 1).astype(jnp.int32)
    live = ((role < jnp.minimum(capacity[own], capacity[partner])) & inside).astype(jnp.int32)
    bits = (jax.random.randint(jax.random.fold_in(key, 13), (SLOTS, blocks, BLOCK, BLOCK), 0, 8) == 0).astype(jnp.int32)
    slot_index = jnp.arange(SLOTS, dtype=jnp.int32)[:, None]
    lower = jnp.minimum(own, partner)
    picked = bits[slot_index, lower]
    tiles = jnp.where((own < partner)[:, :, None, None], picked, jnp.swapaxes(picked, 2, 3))
    tiles = tiles * live[:, :, None, None]
    rows = jnp.transpose(tiles, (1, 2, 0, 3)).reshape(nodes, SLOTS, BLOCK)
    cols = jnp.repeat(jnp.transpose(partner), BLOCK, axis=0)
    return (rows, cols)


def draw_tile_rows(key, part):
    return adjacency_parts(key)[0]


def draw_tile_cols(key, part):
    return adjacency_parts(key)[1]


def plant(values, rng, smallest, largest):
    extent = values.shape
    index_at = [jax.random.randint(jax.random.fold_in(rng, axis), (), 0, extent[axis]) for axis in range(len(extent))]
    values = values.at[tuple(index_at)].set(smallest)
    longest = extent.index(max(extent))
    index_at[longest] = (index_at[longest] + 1) % extent[longest]
    return values.at[tuple(index_at)].set(largest)


def block_scale(stream_key, extent, split, low, high):
    factor_of, own = 1.0, jax.random.fold_in(stream_key, 6)
    for dim, parts in split:
        draws = jnp.exp(jax.random.uniform(jax.random.fold_in(own, dim), (parts,), jnp.float32, low / len(split), high / len(split)))
        factor_of = factor_of * jnp.repeat(draws, extent[dim] // parts).reshape([-1 if axis == dim else 1 for axis in range(len(extent))])
    return factor_of


def scatter_about(own_key, extent, scale, limit, cuts=(), held_as=jnp.bfloat16):
    values = scale * jax.random.normal(own_key, extent, jnp.float32)
    if cuts:
        values = values * block_scale(own_key, extent, cuts, -0.22, 0.18)
    return jnp.clip(values, -limit, limit).astype(held_as)


def setup_inputs(seed: int = 0) -> dict:
    key_of = jax.random.split(jax.random.key(seed), 8)
    features = scatter_about(key_of[0], (NODES, WIDTH), 1.0, 6.0, ((0, 192), (1, 4)))
    out_grad = scatter_about(key_of[1], (NODES, WIDTH), 1.0, 6.0, ((0, 192), (1, 4)))
    self_weight = scatter_about(key_of[2], (WIDTH, WIDTH), WIDTH ** -0.5, 0.25)
    neigh_weight = scatter_about(key_of[3], (WIDTH, WIDTH), (WIDTH // 16) ** -0.5, 1.0)
    tile_rows = draw_tile_rows(jax.random.fold_in(key_of[7], 71), 0)
    tile_cols = draw_tile_cols(jax.random.fold_in(key_of[7], 71), 0)
    degree = plant(jax.random.randint(key_of[6], (NODES,), max(1, SLOTS * BLOCK // 64), SLOTS * BLOCK // 4 + 1), jax.random.fold_in(key_of[6], 1), max(1, SLOTS * BLOCK // 64), (SLOTS * BLOCK // 4 + 1) - 1).astype(jnp.int32)
    return dict(features=features, out_grad=out_grad, self_weight=self_weight, neigh_weight=neigh_weight, tile_rows=tile_rows, tile_cols=tile_cols, degree=degree)


def reference(features, out_grad, self_weight, neigh_weight, tile_rows, tile_cols, degree):
    nodes, width = features.shape
    blocks = nodes // BLOCK
    inverse = 1.0 / degree.astype(jnp.float32)
    scaled = (out_grad.astype(jnp.float32) * inverse[:, None]).astype(jnp.bfloat16)
    feat_blocks = features.reshape(blocks, BLOCK, width)
    grad_blocks = scaled.reshape(blocks, BLOCK, width)

    def one_block(index):
        first = (index * BLOCK).astype(jnp.int32)
        rows = lax.dynamic_slice_in_dim(tile_rows, first, BLOCK, 0).astype(jnp.float32)
        cols = lax.dynamic_index_in_dim(tile_cols, first, 0, keepdims=False)
        feat_panel = feat_blocks[cols].astype(jnp.float32)
        grad_panel = grad_blocks[cols].astype(jnp.float32)
        feat_sum = jnp.einsum("ikj,kjw->iw", rows, feat_panel, precision=lax.Precision.HIGHEST)
        grad_sum = jnp.einsum("ikj,kjw->iw", rows, grad_panel, precision=lax.Precision.HIGHEST)
        return feat_sum, grad_sum

    feat_sum, grad_sum = lax.map(one_block, jnp.arange(blocks, dtype=jnp.int32))
    aggregated = (feat_sum.reshape(nodes, width) * inverse[:, None]).astype(jnp.bfloat16)
    back_agg = grad_sum.reshape(nodes, width).astype(jnp.bfloat16)
    output = jnp.dot(features, self_weight, preferred_element_type=jnp.float32) + jnp.dot(aggregated, neigh_weight, preferred_element_type=jnp.float32)
    feature_grad = jnp.dot(out_grad, self_weight.T, preferred_element_type=jnp.float32) + jnp.dot(back_agg, neigh_weight.T, preferred_element_type=jnp.float32)
    return output.astype(jnp.bfloat16), feature_grad.astype(jnp.bfloat16)
```

```python
import jax
import jax.numpy as jnp
from jax import lax
from jax.sharding import PartitionSpec as P

USE_ALL_TO_ALL = True


def shifted(block, axis, distance):
    devices = range(lax.axis_size(axis))
    route = [(i - distance, i) for i in devices if i - distance in devices]
    return lax.ppermute(block, axis, route)


def swap_chunks(block, axis):
    n = lax.axis_size(axis)
    if USE_ALL_TO_ALL:
        return lax.all_to_all(block, axis, 0, 0, tiled=True)
    m = block.shape[0] // n
    me = lax.axis_index(axis)
    chunks = block.reshape(n, m, block.shape[1])
    got = [None] * n
    got[0] = lax.dynamic_index_in_dim(chunks, me, 0, keepdims=False)
    for s in range(1, n):
        send = lax.dynamic_index_in_dim(chunks, (me + s) % n, 0, keepdims=False)
        got[s] = lax.ppermute(send, axis, [(i, (i + s) % n) for i in range(n)])
    stacked = jnp.stack(got, 0)
    order = (me - jnp.arange(n)) % n
    return jnp.zeros_like(stacked).at[order].set(stacked).reshape(block.shape)


def per_device(features, out_grad, self_weight, neigh_weight, tile_rows, tile_cols, degree):
    rows_here, part = features.shape
    block = tile_rows.shape[2]
    width = self_weight.shape[0]
    n_col = lax.axis_size("col")
    chunk = rows_here // n_col
    inverse = 1.0 / degree.astype(jnp.float32)
    scaled = (out_grad.astype(jnp.float32) * inverse[:, None]).astype(jnp.bfloat16)

    own_in = swap_chunks(jnp.concatenate([features, out_grad], axis=1), "col")

    reach = 2 * block
    pair = jnp.concatenate([features, scaled], axis=1)
    from_prev = shifted(pair[rows_here - reach:], "row", 1)
    from_next = shifted(pair[:reach], "row", -1)
    window = jnp.concatenate([from_prev, pair, from_next], axis=0)
    window_blocks = window.shape[0] // block
    first_block = lax.axis_index("row") * (rows_here // block) - reach // block
    local_cols = tile_cols - first_block
    owner = (
        local_cols[:, :, None] == jnp.arange(window_blocks, dtype=jnp.int32)[None, None, :]
    ).astype(jnp.bfloat16)
    slab = jnp.einsum(
        "rkn,rkb->rnb", owner, tile_rows.astype(jnp.bfloat16), preferred_element_type=jnp.float32
    )
    slab = slab.astype(jnp.bfloat16).reshape(rows_here, window_blocks * block)
    sums = jnp.dot(slab, window, preferred_element_type=jnp.float32)
    aggregated = (sums[:, :part] * inverse[:, None]).astype(jnp.bfloat16)
    back_agg = sums[:, part:].astype(jnp.bfloat16)
    agg_in = swap_chunks(jnp.concatenate([aggregated, back_agg], axis=1), "col")

    own_in = own_in.reshape(n_col, chunk, 2, part)
    agg_in = agg_in.reshape(n_col, chunk, 2, part)
    ws = self_weight.reshape(n_col, part, width)
    wn = neigh_weight.reshape(n_col, part, width)
    ws_t = self_weight.T.reshape(n_col, part, width)
    wn_t = neigh_weight.T.reshape(n_col, part, width)

    def project(x, w):
        return lax.dot_general(
            x, w, (((0, 2), (0, 1)), ((), ())), preferred_element_type=jnp.float32
        )

    output = project(own_in[:, :, 0], ws) + project(agg_in[:, :, 0], wn)
    feature_grad = project(own_in[:, :, 1], ws_t) + project(agg_in[:, :, 1], wn_t)
    both = jnp.stack(
        [output.astype(jnp.bfloat16), feature_grad.astype(jnp.bfloat16)], axis=0
    )
    both = both.reshape(2, chunk, n_col, part).transpose(2, 1, 0, 3).reshape(n_col * chunk, 2 * part)
    back = swap_chunks(both, "col").reshape(rows_here, 2, part)
    return (back[:, 0], back[:, 1])


def solution(mesh):
    placed = (
        P("row", "col"),
        P("row", "col"),
        P(),
        P(),
        P("row", None, None),
        P("row", None),
        P("row"),
    )
    return jax.shard_map(
        per_device,
        mesh=mesh,
        in_specs=placed,
        out_specs=(P("row", "col"), P("row", "col")),
        check_vma=False,
    )
```

```python
import jax
import jax.numpy as jnp
from jax import lax
from jax.sharding import PartitionSpec as P

USE_ALL_TO_ALL = False


def shifted(block, axis, distance):
    devices = range(lax.axis_size(axis))
    route = [(i - distance, i) for i in devices if i - distance in devices]
    return lax.ppermute(block, axis, route)


def swap_chunks(block, axis):
    n = lax.axis_size(axis)
    if USE_ALL_TO_ALL:
        return lax.all_to_all(block, axis, 0, 0, tiled=True)
    m = block.shape[0] // n
    me = lax.axis_index(axis)
    chunks = block.reshape(n, m, block.shape[1])
    got = [lax.dynamic_index_in_dim(chunks, me, 0, keepdims=False)]
    for s in range(1, n):
        send = lax.dynamic_index_in_dim(chunks, (me - s) % n, 0, keepdims=False)
        got.append(lax.ppermute(send, axis, [(i, (i - s) % n) for i in range(n)]))
    stacked = jnp.stack(got, 0)
    return jnp.roll(stacked, me, axis=0).reshape(block.shape)


def per_device(features, out_grad, self_weight, neigh_weight, tile_rows, tile_cols, degree):
    rows_here, part = features.shape
    block = tile_rows.shape[2]
    width = self_weight.shape[0]
    n_col = lax.axis_size("col")
    chunk = rows_here // n_col
    inverse = 1.0 / degree.astype(jnp.float32)
    scaled = (out_grad.astype(jnp.float32) * inverse[:, None]).astype(jnp.bfloat16)

    own_in = swap_chunks(jnp.concatenate([features, out_grad], axis=1), "col")

    reach = 2 * block
    pair = jnp.concatenate([features, scaled], axis=1)
    from_prev = shifted(pair[rows_here - reach:], "row", 1)
    from_next = shifted(pair[:reach], "row", -1)
    window = jnp.concatenate([from_prev, pair, from_next], axis=0)
    window_blocks = window.shape[0] // block
    first_block = lax.axis_index("row") * (rows_here // block) - reach // block
    local_cols = tile_cols - first_block
    owner = (
        local_cols[:, :, None] == jnp.arange(window_blocks, dtype=jnp.int32)[None, None, :]
    ).astype(jnp.bfloat16)
    slab = jnp.einsum(
        "rkn,rkb->rnb", owner, tile_rows.astype(jnp.bfloat16), preferred_element_type=jnp.float32
    )
    slab = slab.astype(jnp.bfloat16).reshape(rows_here, window_blocks * block)
    sums = jnp.dot(slab, window, preferred_element_type=jnp.float32)
    aggregated = (sums[:, :part] * inverse[:, None]).astype(jnp.bfloat16)
    back_agg = sums[:, part:].astype(jnp.bfloat16)
    agg_in = swap_chunks(jnp.concatenate([aggregated, back_agg], axis=1), "col")

    own_in = own_in.reshape(n_col, chunk, 2, part)
    agg_in = agg_in.reshape(n_col, chunk, 2, part)
    ws = self_weight.reshape(n_col, part, width)
    wn = neigh_weight.reshape(n_col, part, width)
    ws_t = self_weight.T.reshape(n_col, part, width)
    wn_t = neigh_weight.T.reshape(n_col, part, width)

    def project(x, w):
        return lax.dot_general(
            x, w, (((0, 2), (0, 1)), ((), ())), preferred_element_type=jnp.float32
        )

    output = project(own_in[:, :, 0], ws) + project(agg_in[:, :, 0], wn)
    feature_grad = project(own_in[:, :, 1], ws_t) + project(agg_in[:, :, 1], wn_t)
    both = jnp.stack(
        [output.astype(jnp.bfloat16), feature_grad.astype(jnp.bfloat16)], axis=0
    )
    both = both.reshape(2, chunk, n_col, part).transpose(2, 1, 0, 3).reshape(n_col * chunk, 2 * part)
    back = swap_chunks(both, "col").reshape(rows_here, 2, part)
    return (back[:, 0], back[:, 1])


def solution(mesh):
    placed = (
        P("row", "col"),
        P("row", "col"),
        P(),
        P(),
        P("row", None, None),
        P("row", None),
        P("row"),
    )
    return jax.shard_map(
        per_device,
        mesh=mesh,
        in_specs=placed,
        out_specs=(P("row", "col"), P("row", "col")),
        check_vma=False,
    )
```

```python
import jax
import jax.numpy as jnp
from jax import lax
from jax.sharding import PartitionSpec as P

USE_ALL_TO_ALL = True


def shifted(block, axis, distance):
    devices = range(lax.axis_size(axis))
    route = [(i - distance, i) for i in devices if i - distance in devices]
    return lax.ppermute(block, axis, route)


def swap_chunks(block, axis):
    n = lax.axis_size(axis)
    if USE_ALL_TO_ALL:
        return lax.all_to_all(block, axis, 0, 0, tiled=True)
    m = block.shape[0] // n
    me = lax.axis_index(axis)
    chunks = block.reshape(n, m, block.shape[1])
    got = [lax.dynamic_index_in_dim(chunks, me, 0, keepdims=False)]
    for s in range(1, n):
        send = lax.dynamic_index_in_dim(chunks, (me - s) % n, 0, keepdims=False)
        got.append(lax.ppermute(send, axis, [(i, (i - s) % n) for i in range(n)]))
    stacked = jnp.stack(got, 0)
    return jnp.roll(stacked, me, axis=0).reshape(block.shape)


def per_device(features, out_grad, self_weight, neigh_weight, tile_rows, tile_cols, degree):
    rows_here, part = features.shape
    block = tile_rows.shape[2]
    width = self_weight.shape[0]
    n_col = lax.axis_size("col")
    chunk = rows_here // n_col
    inverse = 1.0 / degree.astype(jnp.float32)
    scaled = (out_grad.astype(jnp.float32) * inverse[:, None]).astype(jnp.bfloat16)

    reach = 2 * block
    pair = jnp.concatenate([features, scaled], axis=1)
    from_prev = shifted(pair[rows_here - reach:], "row", 1)
    from_next = shifted(pair[:reach], "row", -1)
    window = jnp.concatenate([from_prev, pair, from_next], axis=0)
    window_blocks = window.shape[0] // block
    first_block = lax.axis_index("row") * (rows_here // block) - reach // block
    local_cols = tile_cols - first_block
    owner = (
        local_cols[:, :, None] == jnp.arange(window_blocks, dtype=jnp.int32)[None, None, :]
    ).astype(jnp.bfloat16)
    slab = jnp.einsum(
        "rkn,rkb->rnb", owner, tile_rows.astype(jnp.bfloat16), preferred_element_type=jnp.float32
    )
    slab = slab.astype(jnp.bfloat16).reshape(rows_here, window_blocks * block)
    sums = jnp.dot(slab, window, preferred_element_type=jnp.float32)
    aggregated = (sums[:, :part] * inverse[:, None]).astype(jnp.bfloat16)
    back_agg = sums[:, part:].astype(jnp.bfloat16)
    ins = swap_chunks(
        jnp.concatenate([features, out_grad, aggregated, back_agg], axis=1), "col"
    ).reshape(n_col, chunk, 4, part)
    own_in = ins[:, :, :2]
    agg_in = ins[:, :, 2:]
    ws = self_weight.reshape(n_col, part, width)
    wn = neigh_weight.reshape(n_col, part, width)
    ws_t = self_weight.T.reshape(n_col, part, width)
    wn_t = neigh_weight.T.reshape(n_col, part, width)

    def project(x, w):
        return lax.dot_general(
            x, w, (((0, 2), (0, 1)), ((), ())), preferred_element_type=jnp.float32
        )

    output = project(own_in[:, :, 0], ws) + project(agg_in[:, :, 0], wn)
    feature_grad = project(own_in[:, :, 1], ws_t) + project(agg_in[:, :, 1], wn_t)
    both = jnp.stack(
        [output.astype(jnp.bfloat16), feature_grad.astype(jnp.bfloat16)], axis=0
    )
    both = both.reshape(2, chunk, n_col, part).transpose(2, 1, 0, 3).reshape(n_col * chunk, 2 * part)
    back = swap_chunks(both, "col").reshape(rows_here, 2, part)
    return (back[:, 0], back[:, 1])


def solution(mesh):
    placed = (
        P("row", "col"),
        P("row", "col"),
        P(),
        P(),
        P("row", None, None),
        P("row", None),
        P("row"),
    )
    return jax.shard_map(
        per_device,
        mesh=mesh,
        in_specs=placed,
        out_specs=(P("row", "col"), P("row", "col")),
        check_vma=False,
    )
```

```python
import jax
import jax.numpy as jnp
from jax import lax
from jax.sharding import PartitionSpec as P

USE_ALL_TO_ALL = True


def shifted(block, axis, distance):
    devices = range(lax.axis_size(axis))
    route = [(i - distance, i) for i in devices if i - distance in devices]
    return lax.ppermute(block, axis, route)


def swap_chunks(block, axis):
    n = lax.axis_size(axis)
    if USE_ALL_TO_ALL:
        return lax.all_to_all(block, axis, 0, 0, tiled=True)
    m = block.shape[0] // n
    me = lax.axis_index(axis)
    chunks = block.reshape(n, m, block.shape[1])
    got = [lax.dynamic_index_in_dim(chunks, me, 0, keepdims=False)]
    for s in range(1, n):
        send = lax.dynamic_index_in_dim(chunks, (me - s) % n, 0, keepdims=False)
        got.append(lax.ppermute(send, axis, [(i, (i - s) % n) for i in range(n)]))
    stacked = jnp.stack(got, 0)
    return jnp.roll(stacked, me, axis=0).reshape(block.shape)


def per_device(features, out_grad, self_weight, neigh_weight, tile_rows, tile_cols, degree):
    rows_here, part = features.shape
    block = tile_rows.shape[2]
    width = self_weight.shape[0]
    n_col = lax.axis_size("col")
    chunk = rows_here // n_col
    inverse = 1.0 / degree.astype(jnp.float32)
    scaled = (out_grad.astype(jnp.float32) * inverse[:, None]).astype(jnp.bfloat16)

    reach = 2 * block
    pair = jnp.concatenate([features, scaled], axis=1)
    from_prev = shifted(pair[rows_here - reach:], "row", 1)
    from_next = shifted(pair[:reach], "row", -1)
    window = jnp.concatenate([from_prev, pair, from_next], axis=0)
    window_blocks = window.shape[0] // block
    first_block = lax.axis_index("row") * (rows_here // block) - reach // block
    blocks_here = rows_here // block
    local_cols = tile_cols.reshape(blocks_here, block, -1)[:, 0] - first_block
    owner = (
        local_cols[:, :, None] == jnp.arange(window_blocks, dtype=jnp.int32)[None, None, :]
    ).astype(jnp.bfloat16)
    tiles = tile_rows.astype(jnp.bfloat16).reshape(blocks_here, block, -1, block)
    slab = jnp.einsum("akn,arkb->arnb", owner, tiles, preferred_element_type=jnp.float32)
    slab = slab.astype(jnp.bfloat16).reshape(rows_here, window_blocks * block)
    sums = jnp.dot(slab, window, preferred_element_type=jnp.float32)
    aggregated = (sums[:, :part] * inverse[:, None]).astype(jnp.bfloat16)
    back_agg = sums[:, part:].astype(jnp.bfloat16)
    ins = swap_chunks(
        jnp.concatenate([features, out_grad, aggregated, back_agg], axis=1), "col"
    ).reshape(n_col, chunk, 4, part)
    own_in = ins[:, :, :2]
    agg_in = ins[:, :, 2:]
    ws = self_weight.reshape(n_col, part, width)
    wn = neigh_weight.reshape(n_col, part, width)
    ws_t = self_weight.T.reshape(n_col, part, width)
    wn_t = neigh_weight.T.reshape(n_col, part, width)

    def project(x, w):
        return lax.dot_general(
            x, w, (((0, 2), (0, 1)), ((), ())), preferred_element_type=jnp.float32
        )

    output = project(own_in[:, :, 0], ws) + project(agg_in[:, :, 0], wn)
    feature_grad = project(own_in[:, :, 1], ws_t) + project(agg_in[:, :, 1], wn_t)
    both = jnp.stack(
        [output.astype(jnp.bfloat16), feature_grad.astype(jnp.bfloat16)], axis=0
    )
    both = both.reshape(2, chunk, n_col, part).transpose(2, 1, 0, 3).reshape(n_col * chunk, 2 * part)
    back = swap_chunks(both, "col").reshape(rows_here, 2, part)
    return (back[:, 0], back[:, 1])


def solution(mesh):
    placed = (
        P("row", "col"),
        P("row", "col"),
        P(),
        P(),
        P("row", None, None),
        P("row", None),
        P("row"),
    )
    return jax.shard_map(
        per_device,
        mesh=mesh,
        in_specs=placed,
        out_specs=(P("row", "col"), P("row", "col")),
        check_vma=False,
    )
```

```python
import jax
import jax.numpy as jnp
from jax import lax
from jax.sharding import PartitionSpec as P
from jax.experimental import pallas as pl
from jax.experimental.pallas import tpu as pltpu
import os

INTERPRET = bool(os.environ.get("SOL_INTERPRET"))

USE_ALL_TO_ALL = True


def shifted(block, axis, distance):
    devices = range(lax.axis_size(axis))
    route = [(i - distance, i) for i in devices if i - distance in devices]
    return lax.ppermute(block, axis, route)


def swap_chunks(block, axis):
    n = lax.axis_size(axis)
    if USE_ALL_TO_ALL:
        return lax.all_to_all(block, axis, 0, 0, tiled=True)
    m = block.shape[0] // n
    me = lax.axis_index(axis)
    chunks = block.reshape(n, m, block.shape[1])
    got = [lax.dynamic_index_in_dim(chunks, me, 0, keepdims=False)]
    for s in range(1, n):
        send = lax.dynamic_index_in_dim(chunks, (me - s) % n, 0, keepdims=False)
        got.append(lax.ppermute(send, axis, [(i, (i - s) % n) for i in range(n)]))
    stacked = jnp.stack(got, 0)
    return jnp.roll(stacked, me, axis=0).reshape(block.shape)


def neighbour_sums(local_cols, rows, window, block):
    n_rows, slots, _ = rows.shape
    width = window.shape[1]

    def kernel(cols_ref, rows_ref, win_ref, out_ref):
        a = pl.program_id(0)
        acc = jnp.zeros((block, width), jnp.float32)
        for k in range(slots):
            start = pl.multiple_of(cols_ref[a * slots + k] * block, block)
            tile = rows_ref[:, k, :].astype(jnp.float32).astype(jnp.bfloat16)
            acc += jnp.dot(tile, win_ref[pl.ds(start, block), :], preferred_element_type=jnp.float32)
        out_ref[...] = acc

    return pl.pallas_call(
        kernel,
        out_shape=jax.ShapeDtypeStruct((n_rows, width), jnp.float32),
        grid_spec=pltpu.PrefetchScalarGridSpec(
            num_scalar_prefetch=1,
            grid=(n_rows // block,),
            in_specs=[
                pl.BlockSpec((block, slots, block), lambda a, c: (a, 0, 0)),
                pl.BlockSpec(window.shape, lambda a, c: (0, 0)),
            ],
            out_specs=pl.BlockSpec((block, width), lambda a, c: (a, 0)),
        ),
        interpret=INTERPRET,
    )(local_cols, rows, window)


def per_device(features, out_grad, self_weight, neigh_weight, tile_rows, tile_cols, degree):
    rows_here, part = features.shape
    block = tile_rows.shape[2]
    width = self_weight.shape[0]
    n_col = lax.axis_size("col")
    chunk = rows_here // n_col
    inverse = 1.0 / degree.astype(jnp.float32)
    scaled = (out_grad.astype(jnp.float32) * inverse[:, None]).astype(jnp.bfloat16)

    reach = 2 * block
    pair = jnp.concatenate([features, scaled], axis=1)
    from_prev = shifted(pair[rows_here - reach:], "row", 1)
    from_next = shifted(pair[:reach], "row", -1)
    window = jnp.concatenate([from_prev, pair, from_next], axis=0)
    window_blocks = window.shape[0] // block
    first_block = lax.axis_index("row") * (rows_here // block) - reach // block
    blocks_here = rows_here // block
    local_cols = tile_cols.reshape(blocks_here, block, -1)[:, 0] - first_block
    local_cols = jnp.clip(local_cols, 0, window_blocks - 1).reshape(-1)
    sums = neighbour_sums(local_cols, tile_rows, window, block)
    aggregated = (sums[:, :part] * inverse[:, None]).astype(jnp.bfloat16)
    back_agg = sums[:, part:].astype(jnp.bfloat16)
    ins = swap_chunks(
        jnp.concatenate([features, out_grad, aggregated, back_agg], axis=1), "col"
    ).reshape(n_col, chunk, 4, part)
    own_in = ins[:, :, :2]
    agg_in = ins[:, :, 2:]
    ws = self_weight.reshape(n_col, part, width)
    wn = neigh_weight.reshape(n_col, part, width)
    ws_t = self_weight.T.reshape(n_col, part, width)
    wn_t = neigh_weight.T.reshape(n_col, part, width)

    def project(x, w):
        return lax.dot_general(
            x, w, (((0, 2), (0, 1)), ((), ())), preferred_element_type=jnp.float32
        )

    output = project(own_in[:, :, 0], ws) + project(agg_in[:, :, 0], wn)
    feature_grad = project(own_in[:, :, 1], ws_t) + project(agg_in[:, :, 1], wn_t)
    both = jnp.stack(
        [output.astype(jnp.bfloat16), feature_grad.astype(jnp.bfloat16)], axis=0
    )
    both = both.reshape(2, chunk, n_col, part).transpose(2, 1, 0, 3).reshape(n_col * chunk, 2 * part)
    back = swap_chunks(both, "col").reshape(rows_here, 2, part)
    return (back[:, 0], back[:, 1])


def solution(mesh):
    placed = (
        P("row", "col"),
        P("row", "col"),
        P(),
        P(),
        P("row", None, None),
        P("row", None),
        P("row"),
    )
    return jax.shard_map(
        per_device,
        mesh=mesh,
        in_specs=placed,
        out_specs=(P("row", "col"), P("row", "col")),
        check_vma=False,
    )
```

```python
import jax
import jax.numpy as jnp
from jax import lax
from jax.sharding import PartitionSpec as P
from jax.experimental.layout import Layout, with_layout_constraint

USE_ALL_TO_ALL = True


def shifted(block, axis, distance):
    devices = range(lax.axis_size(axis))
    route = [(i - distance, i) for i in devices if i - distance in devices]
    return lax.ppermute(block, axis, route)


def swap_chunks(block, axis):
    n = lax.axis_size(axis)
    if USE_ALL_TO_ALL:
        return lax.all_to_all(block, axis, 0, 0, tiled=True)
    m = block.shape[0] // n
    me = lax.axis_index(axis)
    chunks = block.reshape(n, m, block.shape[1])
    got = [lax.dynamic_index_in_dim(chunks, me, 0, keepdims=False)]
    for s in range(1, n):
        send = lax.dynamic_index_in_dim(chunks, (me - s) % n, 0, keepdims=False)
        got.append(lax.ppermute(send, axis, [(i, (i - s) % n) for i in range(n)]))
    stacked = jnp.stack(got, 0)
    return jnp.roll(stacked, me, axis=0).reshape(block.shape)


def per_device(features, out_grad, self_weight, neigh_weight, tile_rows, tile_cols, degree):
    rows_here, part = features.shape
    block = tile_rows.shape[2]
    width = self_weight.shape[0]
    n_col = lax.axis_size("col")
    chunk = rows_here // n_col
    inverse = 1.0 / degree.astype(jnp.float32)
    scaled = (out_grad.astype(jnp.float32) * inverse[:, None]).astype(jnp.bfloat16)

    reach = 2 * block
    pair = jnp.concatenate([features, scaled], axis=1)
    from_prev = shifted(pair[rows_here - reach:], "row", 1)
    from_next = shifted(pair[:reach], "row", -1)
    window = jnp.concatenate([from_prev, pair, from_next], axis=0)
    window = with_layout_constraint(window, Layout(major_to_minor=(0, 1)))
    window_blocks = window.shape[0] // block
    first_block = lax.axis_index("row") * (rows_here // block) - reach // block
    blocks_here = rows_here // block
    local_cols = tile_cols.reshape(blocks_here, block, -1)[:, 0] - first_block
    owner = (
        local_cols[:, :, None] == jnp.arange(window_blocks, dtype=jnp.int32)[None, None, :]
    ).astype(jnp.bfloat16)
    tiles = tile_rows.astype(jnp.bfloat16).reshape(blocks_here, block, -1, block)
    slab = jnp.einsum("akn,arkb->arnb", owner, tiles, preferred_element_type=jnp.float32)
    slab = slab.astype(jnp.bfloat16).reshape(rows_here, window_blocks * block)
    sums = jnp.dot(slab, window, preferred_element_type=jnp.float32)
    aggregated = (sums[:, :part] * inverse[:, None]).astype(jnp.bfloat16)
    back_agg = sums[:, part:].astype(jnp.bfloat16)
    ins = swap_chunks(
        jnp.concatenate([features, out_grad, aggregated, back_agg], axis=1), "col"
    ).reshape(n_col, chunk, 4, part)
    own_in = ins[:, :, :2]
    agg_in = ins[:, :, 2:]
    ws = self_weight.reshape(n_col, part, width)
    wn = neigh_weight.reshape(n_col, part, width)
    ws_t = self_weight.T.reshape(n_col, part, width)
    wn_t = neigh_weight.T.reshape(n_col, part, width)

    def project(x, w):
        return lax.dot_general(
            x, w, (((0, 2), (0, 1)), ((), ())), preferred_element_type=jnp.float32
        )

    output = project(own_in[:, :, 0], ws) + project(agg_in[:, :, 0], wn)
    feature_grad = project(own_in[:, :, 1], ws_t) + project(agg_in[:, :, 1], wn_t)
    both = jnp.stack(
        [output.astype(jnp.bfloat16), feature_grad.astype(jnp.bfloat16)], axis=0
    )
    both = both.reshape(2, chunk, n_col, part).transpose(2, 1, 0, 3).reshape(n_col * chunk, 2 * part)
    back = swap_chunks(both, "col").reshape(rows_here, 2, part)
    return (back[:, 0], back[:, 1])


def solution(mesh):
    placed = (
        P("row", "col"),
        P("row", "col"),
        P(),
        P(),
        P("row", None, None),
        P("row", None),
        P("row"),
    )
    return jax.shard_map(
        per_device,
        mesh=mesh,
        in_specs=placed,
        out_specs=(P("row", "col"), P("row", "col")),
        check_vma=False,
    )
```

```python
import jax
import jax.numpy as jnp
from jax import lax
from jax.sharding import PartitionSpec as P

USE_ALL_TO_ALL = True


def shifted(block, axis, distance):
    devices = range(lax.axis_size(axis))
    route = [(i - distance, i) for i in devices if i - distance in devices]
    return lax.ppermute(block, axis, route)


def swap_chunks(block, axis):
    n = lax.axis_size(axis)
    if USE_ALL_TO_ALL:
        return lax.all_to_all(block, axis, 0, 0, tiled=True)
    m = block.shape[0] // n
    me = lax.axis_index(axis)
    chunks = block.reshape(n, m, block.shape[1])
    got = [lax.dynamic_index_in_dim(chunks, me, 0, keepdims=False)]
    for s in range(1, n):
        send = lax.dynamic_index_in_dim(chunks, (me - s) % n, 0, keepdims=False)
        got.append(lax.ppermute(send, axis, [(i, (i - s) % n) for i in range(n)]))
    stacked = jnp.stack(got, 0)
    return jnp.roll(stacked, me, axis=0).reshape(block.shape)


def per_device(features, out_grad, self_weight, neigh_weight, tile_rows, tile_cols, degree):
    rows_here, part = features.shape
    block = tile_rows.shape[2]
    width = self_weight.shape[0]
    n_col = lax.axis_size("col")
    chunk = rows_here // n_col
    inverse = 1.0 / degree.astype(jnp.float32)
    scaled = (out_grad.astype(jnp.float32) * inverse[:, None]).astype(jnp.bfloat16)

    own_in = swap_chunks(jnp.concatenate([features, out_grad], axis=1), "col")

    reach = 2 * block
    pair = jnp.concatenate([features, scaled], axis=1)
    from_prev = shifted(pair[rows_here - reach:], "row", 1)
    from_next = shifted(pair[:reach], "row", -1)
    window = jnp.concatenate([from_prev, pair, from_next], axis=0)
    window_blocks = window.shape[0] // block
    first_block = lax.axis_index("row") * (rows_here // block) - reach // block
    blocks_here = rows_here // block
    local_cols = tile_cols.reshape(blocks_here, block, -1)[:, 0] - first_block
    owner = (
        local_cols[:, :, None] == jnp.arange(window_blocks, dtype=jnp.int32)[None, None, :]
    ).astype(jnp.bfloat16)
    tiles = tile_rows.astype(jnp.bfloat16).reshape(blocks_here, block, -1, block)
    slab = jnp.einsum("akn,arkb->arnb", owner, tiles, preferred_element_type=jnp.float32)
    slab = slab.astype(jnp.bfloat16).reshape(rows_here, window_blocks * block)
    sums = jnp.dot(slab, window, preferred_element_type=jnp.float32)
    aggregated = (sums[:, :part] * inverse[:, None]).astype(jnp.bfloat16)
    back_agg = sums[:, part:].astype(jnp.bfloat16)
    agg_in = swap_chunks(jnp.concatenate([aggregated, back_agg], axis=1), "col")
    own_in = own_in.reshape(n_col, chunk, 2, part)
    agg_in = agg_in.reshape(n_col, chunk, 2, part)
    ws = self_weight.reshape(n_col, part, width)
    wn = neigh_weight.reshape(n_col, part, width)
    ws_t = self_weight.T.reshape(n_col, part, width)
    wn_t = neigh_weight.T.reshape(n_col, part, width)

    def project(x, w):
        return lax.dot_general(
            x, w, (((0, 2), (0, 1)), ((), ())), preferred_element_type=jnp.float32
        )

    output = project(own_in[:, :, 0], ws) + project(agg_in[:, :, 0], wn)
    feature_grad = project(own_in[:, :, 1], ws_t) + project(agg_in[:, :, 1], wn_t)
    both = jnp.stack(
        [output.astype(jnp.bfloat16), feature_grad.astype(jnp.bfloat16)], axis=0
    )
    both = both.reshape(2, chunk, n_col, part).transpose(2, 1, 0, 3).reshape(n_col * chunk, 2 * part)
    back = swap_chunks(both, "col").reshape(rows_here, 2, part)
    return (back[:, 0], back[:, 1])


def solution(mesh):
    placed = (
        P("row", "col"),
        P("row", "col"),
        P(),
        P(),
        P("row", None, None),
        P("row", None),
        P("row"),
    )

    return jax.shard_map(
        per_device,
        mesh=mesh,
        in_specs=placed,
        out_specs=(P("row", "col"), P("row", "col")),
        check_vma=False,
    )
```

```python
import jax
import jax.numpy as jnp
from jax import lax
from jax.sharding import PartitionSpec as P

USE_ALL_TO_ALL = True


def shifted(block, axis, distance):
    devices = range(lax.axis_size(axis))
    route = [(i - distance, i) for i in devices if i - distance in devices]
    return lax.ppermute(block, axis, route)


def swap_chunks(block, axis):
    n = lax.axis_size(axis)
    if USE_ALL_TO_ALL:
        return lax.all_to_all(block, axis, 0, 0, tiled=True)
    m = block.shape[0] // n
    me = lax.axis_index(axis)
    chunks = block.reshape(n, m, block.shape[1])
    got = [lax.dynamic_index_in_dim(chunks, me, 0, keepdims=False)]
    for s in range(1, n):
        send = lax.dynamic_index_in_dim(chunks, (me - s) % n, 0, keepdims=False)
        got.append(lax.ppermute(send, axis, [(i, (i - s) % n) for i in range(n)]))
    stacked = jnp.stack(got, 0)
    return jnp.roll(stacked, me, axis=0).reshape(block.shape)


def per_device(features, out_grad, self_weight, neigh_weight, tile_rows, tile_cols, degree):
    rows_here, part = features.shape
    block = tile_rows.shape[2]
    width = self_weight.shape[0]
    n_col = lax.axis_size("col")
    chunk = rows_here // n_col
    inverse = 1.0 / degree.astype(jnp.float32)
    scaled = (out_grad.astype(jnp.float32) * inverse[:, None]).astype(jnp.bfloat16)

    reach = 2 * block
    pair = jnp.concatenate([features, scaled], axis=1)
    from_prev = shifted(pair[rows_here - reach:], "row", 1)
    from_next = shifted(pair[:reach], "row", -1)
    window = jnp.concatenate([from_prev, pair, from_next], axis=0)
    window_blocks = window.shape[0] // block
    first_block = lax.axis_index("row") * (rows_here // block) - reach // block
    blocks_here = rows_here // block
    local_cols = tile_cols.reshape(blocks_here, block, -1)[:, 0] - first_block
    owner = (
        local_cols[:, :, None] == jnp.arange(window_blocks, dtype=jnp.int32)[None, None, :]
    ).astype(jnp.bfloat16)
    tiles = tile_rows.astype(jnp.bfloat16).reshape(blocks_here, block, -1, block)
    slab = jnp.einsum("akn,arkb->arnb", owner, tiles, preferred_element_type=jnp.float32)
    slab = slab.astype(jnp.bfloat16).reshape(rows_here, window_blocks * block)
    sums = jnp.dot(slab, window, preferred_element_type=jnp.float32)
    aggregated = (sums[:, :part] * inverse[:, None]).astype(jnp.bfloat16)
    back_agg = sums[:, part:].astype(jnp.bfloat16)
    ins = swap_chunks(
        jnp.concatenate([features, out_grad, aggregated, back_agg], axis=1), "col"
    ).reshape(n_col, chunk, 4, part)
    own_in = ins[:, :, :2]
    agg_in = ins[:, :, 2:]
    ws = self_weight.reshape(n_col, part, width)
    wn = neigh_weight.reshape(n_col, part, width)
    ws_t = self_weight.T.reshape(n_col, part, width)
    wn_t = neigh_weight.T.reshape(n_col, part, width)

    def project(x, w):
        return lax.dot_general(
            x, w, (((0, 2), (0, 1)), ((), ())), preferred_element_type=jnp.float32
        )

    output = project(own_in[:, :, 0], ws) + project(agg_in[:, :, 0], wn)
    feature_grad = project(own_in[:, :, 1], ws_t) + project(agg_in[:, :, 1], wn_t)
    both = jnp.stack(
        [output.astype(jnp.bfloat16), feature_grad.astype(jnp.bfloat16)], axis=0
    )
    both = both.reshape(2, chunk, n_col, part).transpose(2, 0, 1, 3)
    back = lax.all_to_all(both, "col", 0, 0, tiled=True)
    return (back[:, 0].reshape(rows_here, part), back[:, 1].reshape(rows_here, part))


def solution(mesh):
    placed = (
        P("row", "col"),
        P("row", "col"),
        P(),
        P(),
        P("row", None, None),
        P("row", None),
        P("row"),
    )
    return jax.shard_map(
        per_device,
        mesh=mesh,
        in_specs=placed,
        out_specs=(P("row", "col"), P("row", "col")),
        check_vma=False,
    )
```

```python
import jax
import jax.numpy as jnp
from jax import lax
from jax.sharding import PartitionSpec as P

USE_ALL_TO_ALL = True


def shifted(block, axis, distance):
    devices = range(lax.axis_size(axis))
    route = [(i - distance, i) for i in devices if i - distance in devices]
    return lax.ppermute(block, axis, route)


def swap_chunks(block, axis):
    n = lax.axis_size(axis)
    if USE_ALL_TO_ALL:
        return lax.all_to_all(block, axis, 0, 0, tiled=True)
    m = block.shape[0] // n
    me = lax.axis_index(axis)
    chunks = block.reshape(n, m, block.shape[1])
    got = [lax.dynamic_index_in_dim(chunks, me, 0, keepdims=False)]
    for s in range(1, n):
        send = lax.dynamic_index_in_dim(chunks, (me - s) % n, 0, keepdims=False)
        got.append(lax.ppermute(send, axis, [(i, (i - s) % n) for i in range(n)]))
    stacked = jnp.stack(got, 0)
    return jnp.roll(stacked, me, axis=0).reshape(block.shape)


def per_device(features, out_grad, self_weight, neigh_weight, tile_rows, tile_cols, degree):
    rows_here, part = features.shape
    block = tile_rows.shape[2]
    width = self_weight.shape[0]
    n_col = lax.axis_size("col")
    chunk = rows_here // n_col
    inverse = 1.0 / degree.astype(jnp.float32)
    scaled = (out_grad.astype(jnp.float32) * inverse[:, None]).astype(jnp.bfloat16)

    reach = 2 * block
    pair = jnp.concatenate([features, scaled], axis=1)
    from_prev = shifted(pair[rows_here - reach:], "row", 1)
    from_next = shifted(pair[:reach], "row", -1)
    window = jnp.concatenate([from_prev, pair, from_next], axis=0)
    window_blocks = window.shape[0] // block
    first_block = lax.axis_index("row") * (rows_here // block) - reach // block
    blocks_here = rows_here // block
    local_cols = tile_cols.reshape(blocks_here, block, -1)[:, 0] - first_block
    owner = (
        local_cols[:, :, None] == jnp.arange(window_blocks, dtype=jnp.int32)[None, None, :]
    ).astype(jnp.bfloat16)
    tiles = tile_rows.astype(jnp.bfloat16).reshape(blocks_here, block, -1, block)
    slab = jnp.einsum("akn,arkb->arnb", owner, tiles, preferred_element_type=jnp.float32)
    slab = slab.astype(jnp.bfloat16).reshape(rows_here, window_blocks * block)
    sums = jnp.dot(slab, window, preferred_element_type=jnp.float32)
    aggregated = (sums[:, :part] * inverse[:, None]).astype(jnp.bfloat16)
    back_agg = sums[:, part:].astype(jnp.bfloat16)
    ins = jnp.stack([features, out_grad, aggregated, back_agg], axis=0)
    ins = ins.reshape(4, n_col, chunk, part).transpose(1, 0, 2, 3)
    ins = lax.all_to_all(ins, "col", 0, 0, tiled=True)
    own_in = ins[:, :2].transpose(0, 2, 1, 3)
    agg_in = ins[:, 2:].transpose(0, 2, 1, 3)
    ws = self_weight.reshape(n_col, part, width)
    wn = neigh_weight.reshape(n_col, part, width)
    ws_t = self_weight.T.reshape(n_col, part, width)
    wn_t = neigh_weight.T.reshape(n_col, part, width)

    def project(x, w):
        return lax.dot_general(
            x, w, (((0, 2), (0, 1)), ((), ())), preferred_element_type=jnp.float32
        )

    output = project(own_in[:, :, 0], ws) + project(agg_in[:, :, 0], wn)
    feature_grad = project(own_in[:, :, 1], ws_t) + project(agg_in[:, :, 1], wn_t)
    both = jnp.stack(
        [output.astype(jnp.bfloat16), feature_grad.astype(jnp.bfloat16)], axis=0
    )
    both = both.reshape(2, chunk, n_col, part).transpose(2, 0, 1, 3)
    back = lax.all_to_all(both, "col", 0, 0, tiled=True)
    return (back[:, 0].reshape(rows_here, part), back[:, 1].reshape(rows_here, part))


def solution(mesh):
    placed = (
        P("row", "col"),
        P("row", "col"),
        P(),
        P(),
        P("row", None, None),
        P("row", None),
        P("row"),
    )
    return jax.shard_map(
        per_device,
        mesh=mesh,
        in_specs=placed,
        out_specs=(P("row", "col"), P("row", "col")),
        check_vma=False,
    )
```

```python
import jax
import jax.numpy as jnp
from jax import lax
from jax.sharding import PartitionSpec as P

USE_ALL_TO_ALL = True


def shifted(block, axis, distance):
    devices = range(lax.axis_size(axis))
    route = [(i - distance, i) for i in devices if i - distance in devices]
    return lax.ppermute(block, axis, route)


def swap_chunks(block, axis):
    n = lax.axis_size(axis)
    if USE_ALL_TO_ALL:
        return lax.all_to_all(block, axis, 0, 0, tiled=True)
    m = block.shape[0] // n
    me = lax.axis_index(axis)
    chunks = block.reshape(n, m, block.shape[1])
    got = [lax.dynamic_index_in_dim(chunks, me, 0, keepdims=False)]
    for s in range(1, n):
        send = lax.dynamic_index_in_dim(chunks, (me - s) % n, 0, keepdims=False)
        got.append(lax.ppermute(send, axis, [(i, (i - s) % n) for i in range(n)]))
    stacked = jnp.stack(got, 0)
    return jnp.roll(stacked, me, axis=0).reshape(block.shape)


def per_device(features, out_grad, self_weight, neigh_weight, tile_rows, tile_cols, degree):
    rows_here, part = features.shape
    block = tile_rows.shape[2]
    width = self_weight.shape[0]
    n_col = lax.axis_size("col")
    chunk = rows_here // n_col
    inverse = 1.0 / degree.astype(jnp.float32)
    scaled = (out_grad.astype(jnp.float32) * inverse[:, None]).astype(jnp.bfloat16)

    reach = 2 * block
    pair = jnp.concatenate([features, scaled], axis=1)
    from_prev = shifted(pair[rows_here - reach:], "row", 1)
    from_next = shifted(pair[:reach], "row", -1)
    window = jnp.concatenate([from_prev, pair, from_next], axis=0)
    window_blocks = window.shape[0] // block
    first_block = lax.axis_index("row") * (rows_here // block) - reach // block
    blocks_here = rows_here // block
    local_cols = tile_cols.reshape(blocks_here, block, -1)[:, 0] - first_block
    owner = (
        local_cols[:, :, None] == jnp.arange(window_blocks, dtype=jnp.int32)[None, None, :]
    ).astype(jnp.bfloat16)
    tiles = tile_rows.astype(jnp.bfloat16).reshape(blocks_here, block, -1, block)
    slab = jnp.einsum("akn,arkb->arnb", owner, tiles, preferred_element_type=jnp.float32)
    slab = slab.astype(jnp.bfloat16).reshape(rows_here, window_blocks * block)
    sums = jnp.dot(slab, window, preferred_element_type=jnp.float32)
    aggregated = (sums[:, :part] * inverse[:, None]).astype(jnp.bfloat16)
    back_agg = sums[:, part:].astype(jnp.bfloat16)
    ins = swap_chunks(
        jnp.concatenate([features, out_grad, aggregated, back_agg], axis=1), "col"
    ).reshape(n_col, chunk, 4, part)
    own_in = ins[:, :, :2]
    agg_in = ins[:, :, 2:]
    ws = self_weight.reshape(n_col, part, width)
    wn = neigh_weight.reshape(n_col, part, width)
    ws_t = self_weight.T.reshape(n_col, part, width)
    wn_t = neigh_weight.T.reshape(n_col, part, width)

    def project(x, w):
        return lax.dot_general(
            x, w, (((0, 2), (0, 1)), ((), ())), preferred_element_type=jnp.float32
        )

    def project_both(x, w):
        return lax.dot_general(
            x, w, (((0, 2, 3), (0, 1, 2)), ((), ())), preferred_element_type=jnp.float32
        )

    output = project_both(ins[:, :, 0::2], jnp.stack([ws, wn], axis=1))
    feature_grad = project_both(ins[:, :, 1::2], jnp.stack([ws_t, wn_t], axis=1))
    both = jnp.stack(
        [output.astype(jnp.bfloat16), feature_grad.astype(jnp.bfloat16)], axis=0
    )
    both = both.reshape(2, chunk, n_col, part).transpose(2, 0, 1, 3)
    back = lax.all_to_all(both, "col", 0, 0, tiled=True)
    return (back[:, 0].reshape(rows_here, part), back[:, 1].reshape(rows_here, part))


def solution(mesh):
    placed = (
        P("row", "col"),
        P("row", "col"),
        P(),
        P(),
        P("row", None, None),
        P("row", None),
        P("row"),
    )
    return jax.shard_map(
        per_device,
        mesh=mesh,
        in_specs=placed,
        out_specs=(P("row", "col"), P("row", "col")),
        check_vma=False,
    )
```
